256 devices in a mesh: seq: 64 (over z, x, core), chan: 4 (over y).
Axes of the slice: x: 4, y: 4, z: 8, core: 2. Of those that a mesh axis runs over, the one named last changes fastest.
Arguments:
- query_proj: bfloat16 [16384, 8192], P('seq', 'chan'), may hold values from -6 to 6
- key_proj: bfloat16 [16384, 8192], P('seq', 'chan'), may hold values from -6 to 6
- value_proj: bfloat16 [16384, 8192], P('seq', 'chan'), may hold values from -6 to 6
- filt_taps: float32 [128, 8192], P(None, 'chan'), may hold values from -0.5 to 0.5
- grad_out: bfloat16 [16384, 8192], P('seq', 'chan'), may hold values from -24 to 24
Outputs:
- grad_q: bfloat16 [16384, 8192], P('seq', 'chan')
- grad_k: bfloat16 [16384, 8192], P('seq', 'chan')
- grad_v: bfloat16 [16384, 8192], P('seq', 'chan')
- grad_filt: float32 [128, 8192], P('seq', 'chan')
The draws below stay inside these ranges and needn't reach their ends.
All inputs are finite; a program needn't handle non-finite values.
Results may differ from the reference program's by a relative error of at most 0.005.
Values may be sent and summed in bfloat16 or wider, within the bound.
No kernel may reach another device: no remote copies, remote signals or barrier semaphores. Data moves between devices by JAX's collectives and lax.ppermute only.
A program may use at most 64 MiB of HBM per device.

```python
import jax
import jax.numpy as jnp
from jax import lax

D = 8192
TAPS = 128
TOKENS = 16384


def draw_grad_out(key, part):
    place = jnp.arange(TOKENS, dtype=jnp.float32)[:, None] / max(TOKENS - 1, 1)
    chan_key = jax.random.fold_in(key, 11)
    base_key = jax.random.fold_in(key, 23)
    spread = jax.random.uniform(chan_key, (1, D), jnp.float32, 0.0, 1.0)
    channel = jnp.exp(spread * jnp.log(10.0)) / 3.0
    base = jnp.clip(jax.random.normal(base_key, (TOKENS, D), jnp.float32), -4.0, 4.0)
    ramp = jnp.exp(jnp.log(3.0) * (place - 0.5))
    return (base * ramp * channel).astype(jnp.bfloat16)


def level_of(stream_key, shape, split, smallest, high):
    factor_of, own = 1.0, jax.random.fold_in(stream_key, 6)
    for axis_at, blocks in split:
        draws = jnp.exp(jax.random.uniform(jax.random.fold_in(own, axis_at), (blocks,), jnp.float32, smallest / len(split), high / len(split)))
        factor_of = factor_of * jnp.repeat(draws, shape[axis_at] // blocks).reshape([-1 if axis == axis_at else 1 for axis in range(len(shape))])
    return factor_of


def bell_draw(key, shape, scale, most, cuts=(), kind=jnp.bfloat16):
    gain = level_of(key, shape, cuts, -0.22, 0.18) if cuts else 1.0
    values = jax.random.normal(key, shape, jnp.float32) * scale * gain
    return jnp.minimum(jnp.maximum(values, -most), most).astype(kind)


def setup_inputs(seed: int = 0) -> dict:
    arg_keys = jax.random.split(jax.random.key(seed), 6)
    return {
        "query_proj": bell_draw(arg_keys[0], (TOKENS, D), 1.0, 6.0, ((0, 64), (1, 4))),
        "key_proj": bell_draw(arg_keys[1], (TOKENS, D), 1.0, 6.0, ((0, 64), (1, 4))),
        "value_proj": bell_draw(arg_keys[2], (TOKENS, D), 1.0, 6.0, ((0, 64), (1, 4))),
        "filt_taps": bell_draw(arg_keys[3], (TAPS, D), TAPS ** -0.5, 0.5, ((1, 4),), jnp.float32),
        "grad_out": draw_grad_out(jax.random.fold_in(arg_keys[5], 71), 0),
    }


def reference(query_proj, key_proj, value_proj, filt_taps, grad_out):
    gated = (key_proj.astype(jnp.float32) * value_proj.astype(jnp.float32)).astype(jnp.bfloat16)
    scaled = (grad_out.astype(jnp.float32) * query_proj.astype(jnp.float32)).astype(jnp.bfloat16)
    reach = TAPS - 1
    gated_wide = gated.astype(jnp.float32)
    scaled_wide = scaled.astype(jnp.float32)
    gated_pad = jnp.concatenate([jnp.zeros((reach, D), gated_wide.dtype), gated_wide], 0)
    scaled_pad = jnp.concatenate([scaled_wide, jnp.zeros((reach, D), scaled_wide.dtype)], 0)

    def add_tap(index, carry):
        filtered, backward = carry
        tap = jnp.asarray(index).astype(jnp.int32)
        weight = lax.dynamic_slice_in_dim(filt_taps, tap, 1, 0)
        earlier = lax.dynamic_slice_in_dim(gated_pad, (reach - tap).astype(jnp.int32), TOKENS, 0)
        later = lax.dynamic_slice_in_dim(scaled_pad, tap, TOKENS, 0)
        return (filtered + weight * earlier, backward + weight * later)
    start = jnp.zeros((TOKENS, D), gated_wide.dtype)
    filtered, grad_gated = lax.fori_loop(0, TAPS, add_tap, (start, start))

    def tap_sum(tap):
        earlier = lax.dynamic_slice_in_dim(gated_pad, (reach - tap).astype(jnp.int32), TOKENS, 0)
        return lax.optimization_barrier(jnp.sum(scaled_wide * earlier, 0))
    filt_sum = lax.map(tap_sum, jnp.arange(TAPS, dtype=jnp.int32))
    grad_q = (grad_out.astype(jnp.float32) * filtered).astype(jnp.bfloat16)
    grad_k = (grad_gated * value_proj.astype(jnp.float32)).astype(jnp.bfloat16)
    grad_v = (grad_gated * key_proj.astype(jnp.float32)).astype(jnp.bfloat16)
    grad_rms = jnp.sqrt(jnp.sum(filt_sum * filt_sum) / (TAPS * D) + 1e-06)
    grad_filt = filt_sum * jnp.minimum(1.0, 1.0 / grad_rms)
    return (grad_q, grad_k, grad_v, grad_filt)
```

```python
import jax
import jax.numpy as jnp
from jax import lax
from jax.sharding import PartitionSpec as P


def shifted(block, axis, distance):
    devices = range(lax.axis_size(axis))
    route = [(i - distance, i) for i in devices if i - distance in devices]
    return lax.ppermute(block, axis, route)


def causal_part(padded, filt):
    width = padded.shape[1]
    out = lax.conv_general_dilated(
        padded[None],
        jnp.flip(filt, 0)[:, None, :],
        (1,),
        "VALID",
        dimension_numbers=("NWC", "WIO", "NWC"),
        feature_group_count=width,
        precision=lax.Precision.HIGHEST,
    )
    return out[0]


def anti_part(padded, filt):
    width = padded.shape[1]
    out = lax.conv_general_dilated(
        padded[None],
        filt[:, None, :],
        (1,),
        "VALID",
        dimension_numbers=("NWC", "WIO", "NWC"),
        feature_group_count=width,
        precision=lax.Precision.HIGHEST,
    )
    return out[0]


def corr_part(padded, kernel):
    width = padded.shape[1]
    out = lax.conv_general_dilated(
        padded[None],
        kernel[:, None, :],
        (1,),
        "VALID",
        dimension_numbers=("NWC", "WIO", "NWC"),
        feature_group_count=width,
        precision=lax.Precision.HIGHEST,
    )
    return out[0]


def halving_sum(rows_rev, axis):
    n = lax.axis_size(axis)
    bits = n.bit_length() - 1
    me = lax.axis_index(axis)
    chans = rows_rev.shape[1]
    pair = rows_rev.shape[0] // n
    buf = rows_rev.reshape((2,) * bits + (pair, chans))
    order = [0, 1, 3, 2, 4, 5] if bits == 6 else list(range(bits))
    for b in order:
        dim = bits - 1 - b
        mine = (me >> b) & 1
        keep = lax.dynamic_slice_in_dim(buf, 1 - mine, 1, dim)
        send = lax.dynamic_slice_in_dim(buf, mine, 1, dim)
        route = [(j, j ^ (1 << b)) for j in range(n)]
        buf = keep + lax.ppermute(send, axis, route)
    return jnp.flip(buf.reshape(pair, chans), 0)


def body(query_proj, key_proj, value_proj, filt_taps, grad_out):
    rows, chans = query_proj.shape
    reach = filt_taps.shape[0] - 1
    gated = (key_proj.astype(jnp.float32) * value_proj.astype(jnp.float32)).astype(jnp.bfloat16)
    scaled = (grad_out.astype(jnp.float32) * query_proj.astype(jnp.float32)).astype(jnp.bfloat16)
    before = shifted(gated[rows - reach :], "seq", 1)
    after = shifted(scaled[:reach], "seq", -1)
    gated_pad = jnp.concatenate([before, gated], 0).astype(jnp.float32)
    scaled_pad = jnp.concatenate([scaled, after], 0).astype(jnp.float32)
    local_sum = corr_part(gated_pad, scaled.astype(jnp.float32))
    portion = halving_sum(local_sum, "seq")
    filtered = causal_part(gated_pad, filt_taps)
    grad_q = (grad_out.astype(jnp.float32) * filtered).astype(jnp.bfloat16)
    grad_gated = anti_part(scaled_pad, filt_taps)
    grad_k = (grad_gated * value_proj.astype(jnp.float32)).astype(jnp.bfloat16)
    grad_v = (grad_gated * key_proj.astype(jnp.float32)).astype(jnp.bfloat16)
    entries = filt_taps.shape[0] * chans * lax.axis_size("chan")
    squares = lax.psum(jnp.sum(portion * portion), ("seq", "chan"))
    grad_rms = jnp.sqrt(squares / entries + 1e-06)
    grad_filt = portion * jnp.minimum(1.0, 1.0 / grad_rms)
    return (grad_q, grad_k, grad_v, grad_filt)


def solution(mesh):
    placed = (
        P("seq", "chan"),
        P("seq", "chan"),
        P("seq", "chan"),
        P(None, "chan"),
        P("seq", "chan"),
    )
    return jax.shard_map(
        body,
        mesh=mesh,
        in_specs=placed,
        out_specs=(P("seq", "chan"), P("seq", "chan"), P("seq", "chan"), P("seq", "chan")),
        check_vma=False,
    )
```

```python
import jax
import jax.numpy as jnp
from jax import lax
from jax.sharding import PartitionSpec as P


def shifted(block, axis, distance):
    devices = range(lax.axis_size(axis))
    route = [(i - distance, i) for i in devices if i - distance in devices]
    return lax.ppermute(block, axis, route)


def causal_part(padded, filt):
    width = padded.shape[1]
    out = lax.conv_general_dilated(
        padded[None],
        jnp.flip(filt, 0)[:, None, :],
        (1,),
        "VALID",
        dimension_numbers=("NWC", "WIO", "NWC"),
        feature_group_count=width,
        precision=lax.Precision.HIGHEST,
    )
    return out[0]


def anti_part(padded, filt):
    width = padded.shape[1]
    out = lax.conv_general_dilated(
        padded[None],
        filt[:, None, :],
        (1,),
        "VALID",
        dimension_numbers=("NWC", "WIO", "NWC"),
        feature_group_count=width,
        precision=lax.Precision.HIGHEST,
    )
    return out[0]


def corr_part(padded, kernel):
    width = padded.shape[1]
    out = lax.conv_general_dilated(
        padded[None],
        kernel[:, None, :],
        (1,),
        "VALID",
        dimension_numbers=("NWC", "WIO", "NWC"),
        feature_group_count=width,
        precision=lax.Precision.HIGHEST,
    )
    return out[0]


def group_rounds(axis_bits):
    if axis_bits == 6:
        return [[0], [1, 2], [3, 4, 5]]
    return [[b] for b in range(axis_bits)]


def partner_route(n, mask):
    return [(j, j ^ mask) for j in range(n)]


def scatter_sum(rows_rev, axis, hook):
    n = lax.axis_size(axis)
    bits = n.bit_length() - 1
    me = lax.axis_index(axis)
    chans = rows_rev.shape[1]
    pair = rows_rev.shape[0] // n
    buf = rows_rev.reshape((2,) * bits + (pair, chans))
    for group in group_rounds(bits):
        dims = [bits - 1 - b for b in group]
        own = [1 - ((me >> b) & 1) for b in group]
        def pick(code):
            out = buf
            for dim, b, o in zip(dims, group, own):
                flip = (code >> group.index(b)) & 1
                out = lax.dynamic_slice_in_dim(out, o ^ flip, 1, dim)
            return out
        acc = pick(0)
        for code in range(1, 1 << len(group)):
            mask = 0
            for k, b in enumerate(group):
                if (code >> k) & 1:
                    mask |= 1 << b
            acc = acc + lax.ppermute(pick(code), axis, partner_route(n, mask))
        buf = hook(acc)
    return jnp.flip(buf.reshape(pair, chans), 0)


def total_sum(value, axis, extra, hook):
    for name in (axis, extra):
        n = lax.axis_size(name)
        for group in group_rounds(n.bit_length() - 1):
            acc = value
            for code in range(1, 1 << len(group)):
                mask = 0
                for k, b in enumerate(group):
                    if (code >> k) & 1:
                        mask |= 1 << b
                acc = acc + lax.ppermute(value, name, partner_route(n, mask))
            value = hook(acc)
    return value


def body(query_proj, key_proj, value_proj, filt_taps, grad_out):
    rows, chans = query_proj.shape
    reach = filt_taps.shape[0] - 1
    gated = (key_proj.astype(jnp.float32) * value_proj.astype(jnp.float32)).astype(jnp.bfloat16)
    scaled = (grad_out.astype(jnp.float32) * query_proj.astype(jnp.float32)).astype(jnp.bfloat16)
    before = shifted(gated[rows - reach :], "seq", 1)
    after = shifted(scaled[:reach], "seq", -1)
    gated_pad = jnp.concatenate([before, gated], 0).astype(jnp.float32)
    scaled_pad = jnp.concatenate([scaled, after], 0).astype(jnp.float32)
    local_sum = corr_part(gated_pad, scaled.astype(jnp.float32))
    pieces = 4
    width = chans // pieces
    work = []
    for p in range(pieces):
        cols = slice(p * width, (p + 1) * width)
        work.append(("q", (gated_pad[:, cols], filt_taps[:, cols], grad_out[:, cols])))
    for p in range(pieces):
        cols = slice(p * width, (p + 1) * width)
        work.append(("kv", (scaled_pad[:, cols], filt_taps[:, cols], value_proj[:, cols], key_proj[:, cols])))
    done = {"q": [], "kv": []}

    def run_next(state):
        if not work:
            return state
        kind, args = work.pop(0)
        state, args = lax.optimization_barrier((state, args))
        if kind == "q":
            pad, filt, out = args
            done["q"].append((out.astype(jnp.float32) * causal_part(pad, filt)).astype(jnp.bfloat16))
        else:
            pad, filt, val, key = args
            grad_gated = anti_part(pad, filt)
            done["kv"].append((
                (grad_gated * val.astype(jnp.float32)).astype(jnp.bfloat16),
                (grad_gated * key.astype(jnp.float32)).astype(jnp.bfloat16),
            ))
        return state

    local_sum = run_next(local_sum)
    portion = scatter_sum(local_sum, "seq", run_next)
    entries = filt_taps.shape[0] * chans * lax.axis_size("chan")
    squares = total_sum(jnp.sum(portion * portion).reshape(1, 1), "seq", "chan", run_next)[0, 0]
    while work:
        squares = run_next(squares)
    grad_q = jnp.concatenate(done["q"], 1)
    grad_k = jnp.concatenate([k for k, _ in done["kv"]], 1)
    grad_v = jnp.concatenate([v for _, v in done["kv"]], 1)
    grad_rms = jnp.sqrt(squares / entries + 1e-06)
    grad_filt = portion * jnp.minimum(1.0, 1.0 / grad_rms)
    return (grad_q, grad_k, grad_v, grad_filt)


def solution(mesh):
    placed = (
        P("seq", "chan"),
        P("seq", "chan"),
        P("seq", "chan"),
        P(None, "chan"),
        P("seq", "chan"),
    )
    return jax.shard_map(
        body,
        mesh=mesh,
        in_specs=placed,
        out_specs=(P("seq", "chan"), P("seq", "chan"), P("seq", "chan"), P("seq", "chan")),
        check_vma=False,
    )
```

```python
import jax
import jax.numpy as jnp
from jax import lax
from jax.sharding import PartitionSpec as P


def shifted(block, axis, distance):
    devices = range(lax.axis_size(axis))
    route = [(i - distance, i) for i in devices if i - distance in devices]
    return lax.ppermute(block, axis, route)


def causal_part(padded, filt):
    width = padded.shape[1]
    out = lax.conv_general_dilated(
        padded[None],
        jnp.flip(filt, 0)[:, None, :],
        (1,),
        "VALID",
        dimension_numbers=("NWC", "WIO", "NWC"),
        feature_group_count=width,
        precision=lax.Precision.HIGHEST,
    )
    return out[0]


def anti_part(padded, filt):
    width = padded.shape[1]
    out = lax.conv_general_dilated(
        padded[None],
        filt[:, None, :],
        (1,),
        "VALID",
        dimension_numbers=("NWC", "WIO", "NWC"),
        feature_group_count=width,
        precision=lax.Precision.HIGHEST,
    )
    return out[0]


def corr_part(padded, kernel):
    width = padded.shape[1]
    out = lax.conv_general_dilated(
        padded[None],
        kernel[:, None, :],
        (1,),
        "VALID",
        dimension_numbers=("NWC", "WIO", "NWC"),
        feature_group_count=width,
        precision=lax.Precision.HIGHEST,
    )
    return out[0]


def group_rounds(axis_bits):
    return [[b] for b in range(axis_bits)]


def partner_route(n, mask):
    return [(j, j ^ mask) for j in range(n)]


def scatter_sum(rows_rev, axis, hook):
    n = lax.axis_size(axis)
    bits = n.bit_length() - 1
    me = lax.axis_index(axis)
    chans = rows_rev.shape[1]
    pair = rows_rev.shape[0] // n
    buf = rows_rev.reshape((2,) * bits + (pair, chans))
    for group in group_rounds(bits):
        dims = [bits - 1 - b for b in group]
        own = [1 - ((me >> b) & 1) for b in group]
        def pick(code):
            out = buf
            for dim, b, o in zip(dims, group, own):
                flip = (code >> group.index(b)) & 1
                out = lax.dynamic_slice_in_dim(out, o ^ flip, 1, dim)
            return out
        acc = pick(0)
        for code in range(1, 1 << len(group)):
            mask = 0
            for k, b in enumerate(group):
                if (code >> k) & 1:
                    mask |= 1 << b
            acc = acc + lax.ppermute(pick(code), axis, partner_route(n, mask))
        buf = hook(acc)
    return jnp.flip(buf.reshape(pair, chans), 0)


def total_sum(value, axis, extra, hook):
    for name in (axis, extra):
        n = lax.axis_size(name)
        for group in group_rounds(n.bit_length() - 1):
            acc = value
            for code in range(1, 1 << len(group)):
                mask = 0
                for k, b in enumerate(group):
                    if (code >> k) & 1:
                        mask |= 1 << b
                acc = acc + lax.ppermute(value, name, partner_route(n, mask))
            value = hook(acc)
    return value


def body(query_proj, key_proj, value_proj, filt_taps, grad_out):
    rows, chans = query_proj.shape
    reach = filt_taps.shape[0] - 1
    gated = (key_proj.astype(jnp.float32) * value_proj.astype(jnp.float32)).astype(jnp.bfloat16)
    scaled = (grad_out.astype(jnp.float32) * query_proj.astype(jnp.float32)).astype(jnp.bfloat16)
    before = shifted(gated[rows - reach :], "seq", 1)
    after = shifted(scaled[:reach], "seq", -1)
    gated_pad = jnp.concatenate([before, gated], 0).astype(jnp.float32)
    scaled_pad = jnp.concatenate([scaled, after], 0).astype(jnp.float32)
    local_sum = corr_part(gated_pad, scaled.astype(jnp.float32))
    pieces = 4
    width = chans // pieces
    work = []
    for p in range(pieces):
        cols = slice(p * width, (p + 1) * width)
        work.append(("q", (gated_pad[:, cols], filt_taps[:, cols], grad_out[:, cols])))
    for p in range(pieces):
        cols = slice(p * width, (p + 1) * width)
        work.append(("kv", (scaled_pad[:, cols], filt_taps[:, cols], value_proj[:, cols], key_proj[:, cols])))
    done = {"q": [], "kv": []}

    def run_next(state):
        if not work:
            return state
        kind, args = work.pop(0)
        state, args = lax.optimization_barrier((state, args))
        if kind == "q":
            pad, filt, out = args
            done["q"].append((out.astype(jnp.float32) * causal_part(pad, filt)).astype(jnp.bfloat16))
        else:
            pad, filt, val, key = args
            grad_gated = anti_part(pad, filt)
            done["kv"].append((
                (grad_gated * val.astype(jnp.float32)).astype(jnp.bfloat16),
                (grad_gated * key.astype(jnp.float32)).astype(jnp.bfloat16),
            ))
        return state

    local_sum = run_next(local_sum)
    portion = scatter_sum(local_sum, "seq", run_next)
    entries = filt_taps.shape[0] * chans * lax.axis_size("chan")
    squares = total_sum(jnp.sum(portion * portion).reshape(1, 1), "seq", "chan", run_next)[0, 0]
    while work:
        squares = run_next(squares)
    grad_q = jnp.concatenate(done["q"], 1)
    grad_k = jnp.concatenate([k for k, _ in done["kv"]], 1)
    grad_v = jnp.concatenate([v for _, v in done["kv"]], 1)
    grad_rms = jnp.sqrt(squares / entries + 1e-06)
    grad_filt = portion * jnp.minimum(1.0, 1.0 / grad_rms)
    return (grad_q, grad_k, grad_v, grad_filt)


def solution(mesh):
    placed = (
        P("seq", "chan"),
        P("seq", "chan"),
        P("seq", "chan"),
        P(None, "chan"),
        P("seq", "chan"),
    )
    return jax.shard_map(
        body,
        mesh=mesh,
        in_specs=placed,
        out_specs=(P("seq", "chan"), P("seq", "chan"), P("seq", "chan"), P("seq", "chan")),
        check_vma=False,
    )
```

```python
import jax
import jax.numpy as jnp
from jax import lax
from jax.sharding import PartitionSpec as P


def shifted(block, axis, distance):
    devices = range(lax.axis_size(axis))
    route = [(i - distance, i) for i in devices if i - distance in devices]
    return lax.ppermute(block, axis, route)


def causal_part(padded, filt):
    width = padded.shape[1]
    out = lax.conv_general_dilated(
        padded[None],
        jnp.flip(filt, 0)[:, None, :],
        (1,),
        "VALID",
        dimension_numbers=("NWC", "WIO", "NWC"),
        feature_group_count=width,
        precision=lax.Precision.HIGHEST,
    )
    return out[0]


def anti_part(padded, filt):
    width = padded.shape[1]
    out = lax.conv_general_dilated(
        padded[None],
        filt[:, None, :],
        (1,),
        "VALID",
        dimension_numbers=("NWC", "WIO", "NWC"),
        feature_group_count=width,
        precision=lax.Precision.HIGHEST,
    )
    return out[0]


def corr_part(padded, kernel):
    width = padded.shape[1]
    out = lax.conv_general_dilated(
        padded[None],
        kernel[:, None, :],
        (1,),
        "VALID",
        dimension_numbers=("NWC", "WIO", "NWC"),
        feature_group_count=width,
        precision=lax.Precision.HIGHEST,
    )
    return out[0]


def group_rounds(axis_bits):
    return [[b] for b in range(axis_bits)]


def partner_route(n, mask):
    return [(j, j ^ mask) for j in range(n)]


def scatter_sum(rows_rev, axis, hook):
    n = lax.axis_size(axis)
    bits = n.bit_length() - 1
    me = lax.axis_index(axis)
    chans = rows_rev.shape[1]
    pair = rows_rev.shape[0] // n
    buf = rows_rev.reshape((2,) * bits + (pair, chans))
    for group in group_rounds(bits):
        dims = [bits - 1 - b for b in group]
        own = [1 - ((me >> b) & 1) for b in group]
        def pick(code):
            out = buf
            for dim, b, o in zip(dims, group, own):
                flip = (code >> group.index(b)) & 1
                out = lax.dynamic_slice_in_dim(out, o ^ flip, 1, dim)
            return out
        acc = pick(0)
        for code in range(1, 1 << len(group)):
            mask = 0
            for k, b in enumerate(group):
                if (code >> k) & 1:
                    mask |= 1 << b
            acc = acc + lax.ppermute(pick(code), axis, partner_route(n, mask))
        buf = hook(acc)
    return jnp.flip(buf.reshape(pair, chans), 0)


def total_sum(value, axes):
    n = 1
    for name in axes:
        n *= lax.axis_size(name)
    terms = lax.all_to_all(jnp.broadcast_to(value, (n, 128)), axes, 0, 0, tiled=True)
    return jnp.sum(terms[:, 0])


def body(query_proj, key_proj, value_proj, filt_taps, grad_out):
    rows, chans = query_proj.shape
    reach = filt_taps.shape[0] - 1
    gated = (key_proj.astype(jnp.float32) * value_proj.astype(jnp.float32)).astype(jnp.bfloat16)
    scaled = (grad_out.astype(jnp.float32) * query_proj.astype(jnp.float32)).astype(jnp.bfloat16)
    before = shifted(gated[rows - reach :], "seq", 1)
    after = shifted(scaled[:reach], "seq", -1)
    gated_pad = jnp.concatenate([before, gated], 0).astype(jnp.float32)
    scaled_pad = jnp.concatenate([scaled, after], 0).astype(jnp.float32)
    local_sum = corr_part(gated_pad, scaled.astype(jnp.float32))
    pieces = 4
    width = chans // pieces
    work = []
    for p in range(pieces):
        cols = slice(p * width, (p + 1) * width)
        work.append(("q", (gated_pad[:, cols], filt_taps[:, cols], grad_out[:, cols])))
    for p in range(pieces):
        cols = slice(p * width, (p + 1) * width)
        work.append(("kv", (scaled_pad[:, cols], filt_taps[:, cols], value_proj[:, cols], key_proj[:, cols])))
    done = {"q": [], "kv": []}

    def run_next(state):
        if not work:
            return state
        kind, args = work.pop(0)
        state, args = lax.optimization_barrier((state, args))
        if kind == "q":
            pad, filt, out = args
            done["q"].append((out.astype(jnp.float32) * causal_part(pad, filt)).astype(jnp.bfloat16))
        else:
            pad, filt, val, key = args
            grad_gated = anti_part(pad, filt)
            done["kv"].append((
                (grad_gated * val.astype(jnp.float32)).astype(jnp.bfloat16),
                (grad_gated * key.astype(jnp.float32)).astype(jnp.bfloat16),
            ))
        return state

    local_sum = run_next(local_sum)
    portion = scatter_sum(local_sum, "seq", run_next)
    entries = filt_taps.shape[0] * chans * lax.axis_size("chan")
    while work:
        portion = run_next(portion)
    squares = total_sum(jnp.sum(portion * portion), ("seq", "chan"))
    grad_q = jnp.concatenate(done["q"], 1)
    grad_k = jnp.concatenate([k for k, _ in done["kv"]], 1)
    grad_v = jnp.concatenate([v for _, v in done["kv"]], 1)
    grad_rms = jnp.sqrt(squares / entries + 1e-06)
    grad_filt = portion * jnp.minimum(1.0, 1.0 / grad_rms)
    return (grad_q, grad_k, grad_v, grad_filt)


def solution(mesh):
    placed = (
        P("seq", "chan"),
        P("seq", "chan"),
        P("seq", "chan"),
        P(None, "chan"),
        P("seq", "chan"),
    )
    return jax.shard_map(
        body,
        mesh=mesh,
        in_specs=placed,
        out_specs=(P("seq", "chan"), P("seq", "chan"), P("seq", "chan"), P("seq", "chan")),
        check_vma=False,
    )
```

```python
import jax
import jax.numpy as jnp
from jax import lax
from jax.sharding import PartitionSpec as P


def shifted(block, axis, distance):
    devices = range(lax.axis_size(axis))
    route = [(i - distance, i) for i in devices if i - distance in devices]
    return lax.ppermute(block, axis, route)


def causal_part(padded, filt):
    width = padded.shape[1]
    out = lax.conv_general_dilated(
        padded[None],
        jnp.flip(filt, 0)[:, None, :],
        (1,),
        "VALID",
        dimension_numbers=("NWC", "WIO", "NWC"),
        feature_group_count=width,
        precision=lax.Precision.HIGHEST,
    )
    return out[0]


def anti_part(padded, filt):
    width = padded.shape[1]
    out = lax.conv_general_dilated(
        padded[None],
        filt[:, None, :],
        (1,),
        "VALID",
        dimension_numbers=("NWC", "WIO", "NWC"),
        feature_group_count=width,
        precision=lax.Precision.HIGHEST,
    )
    return out[0]


def corr_part(padded, kernel):
    width = padded.shape[1]
    out = lax.conv_general_dilated(
        padded[None],
        kernel[:, None, :],
        (1,),
        "VALID",
        dimension_numbers=("NWC", "WIO", "NWC"),
        feature_group_count=width,
        precision=lax.Precision.HIGHEST,
    )
    return out[0]


def group_rounds(axis_bits):
    return [[b] for b in range(axis_bits)]


def partner_route(n, mask):
    return [(j, j ^ mask) for j in range(n)]


def scatter_sum(rows_rev, axis, hook):
    n = lax.axis_size(axis)
    bits = n.bit_length() - 1
    me = lax.axis_index(axis)
    chans = rows_rev.shape[1]
    pair = rows_rev.shape[0] // n
    buf = rows_rev.reshape((2,) * bits + (pair, chans))
    for group in group_rounds(bits):
        dims = [bits - 1 - b for b in group]
        own = [1 - ((me >> b) & 1) for b in group]
        def pick(code):
            out = buf
            for dim, b, o in zip(dims, group, own):
                flip = (code >> group.index(b)) & 1
                out = lax.dynamic_slice_in_dim(out, o ^ flip, 1, dim)
            return out
        acc = pick(0)
        for code in range(1, 1 << len(group)):
            mask = 0
            for k, b in enumerate(group):
                if (code >> k) & 1:
                    mask |= 1 << b
            acc = acc + lax.ppermute(pick(code), axis, partner_route(n, mask))
        buf = hook(acc)
    return jnp.flip(buf.reshape(pair, chans), 0)


def total_sum(value, axes):
    n = 1
    for name in axes:
        n *= lax.axis_size(name)
    terms = lax.all_to_all(jnp.broadcast_to(value, (n, 128)), axes, 0, 0, tiled=True)
    return jnp.sum(terms[:, 0])


def body(query_proj, key_proj, value_proj, filt_taps, grad_out):
    rows, chans = query_proj.shape
    reach = filt_taps.shape[0] - 1
    gated = (key_proj.astype(jnp.float32) * value_proj.astype(jnp.float32)).astype(jnp.bfloat16)
    scaled = (grad_out.astype(jnp.float32) * query_proj.astype(jnp.float32)).astype(jnp.bfloat16)
    before = shifted(gated[rows - reach :], "seq", 1)
    after = shifted(scaled[:reach], "seq", -1)
    gated_pad = jnp.concatenate([before, gated], 0).astype(jnp.float32)
    scaled_pad = jnp.concatenate([scaled, after], 0).astype(jnp.float32)
    local_sum = corr_part(gated_pad, scaled.astype(jnp.float32))
    pieces = 4
    width = chans // pieces
    work = [("q", p) for p in range(pieces)] + [("kv", p) for p in range(pieces)]
    whole = (gated_pad, scaled_pad, filt_taps, grad_out, value_proj, key_proj)
    done = {"q": [], "kv": []}

    def run_next(state):
        if not work:
            return state
        kind, p = work.pop(0)
        state, arrays = lax.optimization_barrier((state, whole))
        g_pad, s_pad, filt, out, val, key = arrays
        cols = slice(p * width, (p + 1) * width)
        if kind == "q":
            filtered = causal_part(g_pad[:, cols], filt[:, cols])
            done["q"].append((out[:, cols].astype(jnp.float32) * filtered).astype(jnp.bfloat16))
        else:
            grad_gated = anti_part(s_pad[:, cols], filt[:, cols])
            done["kv"].append((
                (grad_gated * val[:, cols].astype(jnp.float32)).astype(jnp.bfloat16),
                (grad_gated * key[:, cols].astype(jnp.float32)).astype(jnp.bfloat16),
            ))
        return state

    local_sum = run_next(local_sum)
    portion = scatter_sum(local_sum, "seq", run_next)
    entries = filt_taps.shape[0] * chans * lax.axis_size("chan")
    while work:
        portion = run_next(portion)
    squares = total_sum(jnp.sum(portion * portion), ("seq", "chan"))
    grad_q = jnp.concatenate(done["q"], 1)
    grad_k = jnp.concatenate([k for k, _ in done["kv"]], 1)
    grad_v = jnp.concatenate([v for _, v in done["kv"]], 1)
    grad_rms = jnp.sqrt(squares / entries + 1e-06)
    grad_filt = portion * jnp.minimum(1.0, 1.0 / grad_rms)
    return (grad_q, grad_k, grad_v, grad_filt)


def solution(mesh):
    placed = (
        P("seq", "chan"),
        P("seq", "chan"),
        P("seq", "chan"),
        P(None, "chan"),
        P("seq", "chan"),
    )
    return jax.shard_map(
        body,
        mesh=mesh,
        in_specs=placed,
        out_specs=(P("seq", "chan"), P("seq", "chan"), P("seq", "chan"), P("seq", "chan")),
        check_vma=False,
    )
```

```python
import jax
import jax.numpy as jnp
from jax import lax
from jax.sharding import PartitionSpec as P


def shifted(block, axis, distance):
    devices = range(lax.axis_size(axis))
    route = [(i - distance, i) for i in devices if i - distance in devices]
    return lax.ppermute(block, axis, route)


def causal_part(padded, filt):
    width = padded.shape[1]
    out = lax.conv_general_dilated(
        padded[None],
        jnp.flip(filt, 0)[:, None, :],
        (1,),
        "VALID",
        dimension_numbers=("NWC", "WIO", "NWC"),
        feature_group_count=width,
        precision=lax.Precision.HIGHEST,
    )
    return out[0]


def anti_part(padded, filt):
    width = padded.shape[1]
    out = lax.conv_general_dilated(
        padded[None],
        filt[:, None, :],
        (1,),
        "VALID",
        dimension_numbers=("NWC", "WIO", "NWC"),
        feature_group_count=width,
        precision=lax.Precision.HIGHEST,
    )
    return out[0]


def corr_part(padded, kernel):
    width = padded.shape[1]
    out = lax.conv_general_dilated(
        padded[None],
        kernel[:, None, :],
        (1,),
        "VALID",
        dimension_numbers=("NWC", "WIO", "NWC"),
        feature_group_count=width,
        precision=lax.Precision.HIGHEST,
    )
    return out[0]


def group_rounds(axis_bits):
    return [[b] for b in range(axis_bits)]


def partner_route(n, mask):
    return [(j, j ^ mask) for j in range(n)]


def scatter_sum(rows_rev, axis, hook):
    n = lax.axis_size(axis)
    bits = n.bit_length() - 1
    me = lax.axis_index(axis)
    chans = rows_rev.shape[1]
    pair = rows_rev.shape[0] // n
    buf = rows_rev.reshape((2,) * bits + (pair, chans))
    for group in group_rounds(bits):
        dims = [bits - 1 - b for b in group]
        own = [1 - ((me >> b) & 1) for b in group]
        def pick(code):
            out = buf
            for dim, b, o in zip(dims, group, own):
                flip = (code >> group.index(b)) & 1
                out = lax.dynamic_slice_in_dim(out, o ^ flip, 1, dim)
            return out
        acc = pick(0)
        for code in range(1, 1 << len(group)):
            mask = 0
            for k, b in enumerate(group):
                if (code >> k) & 1:
                    mask |= 1 << b
            acc = acc + lax.ppermute(pick(code), axis, partner_route(n, mask))
        buf = hook(acc)
    return jnp.flip(buf.reshape(pair, chans), 0)


def total_sum(value, axes):
    n = 1
    for name in axes:
        n *= lax.axis_size(name)
    terms = lax.all_to_all(jnp.broadcast_to(value, (n, 128)), axes, 0, 0, tiled=True)
    return jnp.sum(terms[:, 0])


def body(query_proj, key_proj, value_proj, filt_taps, grad_out):
    rows, chans = query_proj.shape
    reach = filt_taps.shape[0] - 1
    gated = (key_proj.astype(jnp.float32) * value_proj.astype(jnp.float32)).astype(jnp.bfloat16)
    scaled = (grad_out.astype(jnp.float32) * query_proj.astype(jnp.float32)).astype(jnp.bfloat16)
    before = shifted(gated[rows - reach :], "seq", 1)
    after = shifted(scaled[:reach], "seq", -1)
    pieces = 4
    width = chans // pieces
    spans = [slice(p * width, (p + 1) * width) for p in range(pieces)]
    g_pads = [jnp.concatenate([before[:, c], gated[:, c]], 0).astype(jnp.float32) for c in spans]
    s_pads = [jnp.concatenate([scaled[:, c], after[:, c]], 0).astype(jnp.float32) for c in spans]
    local_sum = jnp.concatenate(
        [corr_part(g_pads[p], scaled[:, c].astype(jnp.float32)) for p, c in enumerate(spans)], 1
    )
    work = [("q", p) for p in range(pieces)] + [("kv", p) for p in range(pieces)]
    done = {"q": [], "kv": []}

    def run_next(state):
        if not work:
            return state
        kind, p = work.pop(0)
        c = spans[p]
        if kind == "q":
            state, pad = lax.optimization_barrier((state, g_pads[p]))
            filtered = causal_part(pad, filt_taps[:, c])
            done["q"].append((grad_out[:, c].astype(jnp.float32) * filtered).astype(jnp.bfloat16))
        else:
            state, pad = lax.optimization_barrier((state, s_pads[p]))
            grad_gated = anti_part(pad, filt_taps[:, c])
            done["kv"].append((
                (grad_gated * value_proj[:, c].astype(jnp.float32)).astype(jnp.bfloat16),
                (grad_gated * key_proj[:, c].astype(jnp.float32)).astype(jnp.bfloat16),
            ))
        return state

    local_sum = run_next(local_sum)
    portion = scatter_sum(local_sum, "seq", run_next)
    entries = filt_taps.shape[0] * chans * lax.axis_size("chan")
    while work:
        portion = run_next(portion)
    squares = total_sum(jnp.sum(portion * portion), ("seq", "chan"))
    grad_q = jnp.concatenate(done["q"], 1)
    grad_k = jnp.concatenate([k for k, _ in done["kv"]], 1)
    grad_v = jnp.concatenate([v for _, v in done["kv"]], 1)
    grad_rms = jnp.sqrt(squares / entries + 1e-06)
    grad_filt = portion * jnp.minimum(1.0, 1.0 / grad_rms)
    return (grad_q, grad_k, grad_v, grad_filt)


def solution(mesh):
    placed = (
        P("seq", "chan"),
        P("seq", "chan"),
        P("seq", "chan"),
        P(None, "chan"),
        P("seq", "chan"),
    )
    return jax.shard_map(
        body,
        mesh=mesh,
        in_specs=placed,
        out_specs=(P("seq", "chan"), P("seq", "chan"), P("seq", "chan"), P("seq", "chan")),
        check_vma=False,
    )
```

```python
import jax
import jax.numpy as jnp
from jax import lax
from jax.sharding import PartitionSpec as P


def shifted(block, axis, distance):
    devices = range(lax.axis_size(axis))
    route = [(i - distance, i) for i in devices if i - distance in devices]
    return lax.ppermute(block, axis, route)


def causal_part(padded, filt):
    width = padded.shape[1]
    out = lax.conv_general_dilated(
        padded[None],
        jnp.flip(filt, 0)[:, None, :],
        (1,),
        "VALID",
        dimension_numbers=("NWC", "WIO", "NWC"),
        feature_group_count=width,
        precision=lax.Precision.HIGHEST,
    )
    return out[0]


def anti_part(padded, filt):
    width = padded.shape[1]
    out = lax.conv_general_dilated(
        padded[None],
        filt[:, None, :],
        (1,),
        "VALID",
        dimension_numbers=("NWC", "WIO", "NWC"),
        feature_group_count=width,
        precision=lax.Precision.HIGHEST,
    )
    return out[0]


def corr_part(padded, kernel):
    width = padded.shape[1]
    out = lax.conv_general_dilated(
        padded[None],
        kernel[:, None, :],
        (1,),
        "VALID",
        dimension_numbers=("NWC", "WIO", "NWC"),
        feature_group_count=width,
        precision=lax.Precision.HIGHEST,
    )
    return out[0]


def group_rounds(axis_bits):
    return [[b] for b in range(axis_bits)]


def partner_route(n, mask):
    return [(j, j ^ mask) for j in range(n)]


def scatter_sum(rows_rev, axis, hook):
    n = lax.axis_size(axis)
    bits = n.bit_length() - 1
    me = lax.axis_index(axis)
    chans = rows_rev.shape[1]
    pair = rows_rev.shape[0] // n
    buf = rows_rev.reshape((2,) * bits + (pair, chans))
    for group in group_rounds(bits):
        dims = [bits - 1 - b for b in group]
        own = [1 - ((me >> b) & 1) for b in group]
        def pick(code):
            out = buf
            for dim, b, o in zip(dims, group, own):
                flip = (code >> group.index(b)) & 1
                out = lax.dynamic_slice_in_dim(out, o ^ flip, 1, dim)
            return out
        acc = pick(0)
        for code in range(1, 1 << len(group)):
            mask = 0
            for k, b in enumerate(group):
                if (code >> k) & 1:
                    mask |= 1 << b
            acc = acc + lax.ppermute(pick(code), axis, partner_route(n, mask))
        buf = hook(acc)
    return jnp.flip(buf.reshape(pair, chans), 0)


def total_sum(value, axes):
    n = 1
    for name in axes:
        n *= lax.axis_size(name)
    terms = lax.all_to_all(jnp.broadcast_to(value, (n, 128)), axes, 0, 0, tiled=True)
    return jnp.sum(terms[:, 0])


def body(query_proj, key_proj, value_proj, filt_taps, grad_out):
    rows, chans = query_proj.shape
    reach = filt_taps.shape[0] - 1
    gated = (key_proj.astype(jnp.float32) * value_proj.astype(jnp.float32)).astype(jnp.bfloat16)
    scaled = (grad_out.astype(jnp.float32) * query_proj.astype(jnp.float32)).astype(jnp.bfloat16)
    before = shifted(gated[rows - reach :], "seq", 1)
    after = shifted(scaled[:reach], "seq", -1)
    gated_pad = jnp.concatenate([before, gated], 0).astype(jnp.float32)
    scaled_pad = jnp.concatenate([scaled, after], 0).astype(jnp.float32)
    local_sum = corr_part(gated_pad, scaled.astype(jnp.float32))
    pieces = 4
    width = chans // pieces
    work = []
    for p in range(pieces):
        cols = slice(p * width, (p + 1) * width)
        work.append(("q", (gated_pad[:, cols], filt_taps[:, cols])))
    for p in range(pieces):
        cols = slice(p * width, (p + 1) * width)
        work.append(("kv", (scaled_pad[:, cols], filt_taps[:, cols])))
    done = {"q": [], "kv": []}

    def run_next(state):
        if not work:
            return state
        kind, args = work.pop(0)
        state, (pad, filt) = lax.optimization_barrier((state, args))
        if kind == "q":
            done["q"].append(causal_part(pad, filt))
        else:
            done["kv"].append(anti_part(pad, filt))
        return state

    local_sum = run_next(local_sum)
    portion = scatter_sum(local_sum, "seq", run_next)
    entries = filt_taps.shape[0] * chans * lax.axis_size("chan")
    while work:
        portion = run_next(portion)
    squares = total_sum(jnp.sum(portion * portion), ("seq", "chan"))
    filtered = jnp.concatenate(done["q"], 1)
    grad_gated = jnp.concatenate(done["kv"], 1)
    grad_q = (grad_out.astype(jnp.float32) * filtered).astype(jnp.bfloat16)
    grad_k = (grad_gated * value_proj.astype(jnp.float32)).astype(jnp.bfloat16)
    grad_v = (grad_gated * key_proj.astype(jnp.float32)).astype(jnp.bfloat16)
    grad_rms = jnp.sqrt(squares / entries + 1e-06)
    grad_filt = portion * jnp.minimum(1.0, 1.0 / grad_rms)
    return (grad_q, grad_k, grad_v, grad_filt)


def solution(mesh):
    placed = (
        P("seq", "chan"),
        P("seq", "chan"),
        P("seq", "chan"),
        P(None, "chan"),
        P("seq", "chan"),
    )
    return jax.shard_map(
        body,
        mesh=mesh,
        in_specs=placed,
        out_specs=(P("seq", "chan"), P("seq", "chan"), P("seq", "chan"), P("seq", "chan")),
        check_vma=False,
    )
```

```python
import jax
import jax.numpy as jnp
from jax import lax
from jax.sharding import PartitionSpec as P


def shifted(block, axis, distance):
    devices = range(lax.axis_size(axis))
    route = [(i - distance, i) for i in devices if i - distance in devices]
    return lax.ppermute(block, axis, route)


def causal_part(padded, filt):
    width = padded.shape[1]
    out = lax.conv_general_dilated(
        padded[None],
        jnp.flip(filt, 0)[:, None, :],
        (1,),
        "VALID",
        dimension_numbers=("NWC", "WIO", "NWC"),
        feature_group_count=width,
        precision=lax.Precision.HIGHEST,
    )
    return out[0]


def anti_part(padded, filt):
    width = padded.shape[1]
    out = lax.conv_general_dilated(
        padded[None],
        filt[:, None, :],
        (1,),
        "VALID",
        dimension_numbers=("NWC", "WIO", "NWC"),
        feature_group_count=width,
        precision=lax.Precision.HIGHEST,
    )
    return out[0]


def corr_part(padded, kernel):
    width = padded.shape[1]
    out = lax.conv_general_dilated(
        padded[None],
        kernel[:, None, :],
        (1,),
        "VALID",
        dimension_numbers=("NWC", "WIO", "NWC"),
        feature_group_count=width,
        precision=lax.Precision.HIGHEST,
    )
    return out[0]


def group_rounds(axis_bits):
    return [[b] for b in range(axis_bits)]


def partner_route(n, mask):
    return [(j, j ^ mask) for j in range(n)]


def scatter_sum(rows_rev, axis, hook):
    n = lax.axis_size(axis)
    bits = n.bit_length() - 1
    me = lax.axis_index(axis)
    chans = rows_rev.shape[1]
    pair = rows_rev.shape[0] // n
    buf = rows_rev.reshape((2,) * bits + (pair, chans))
    for group in group_rounds(bits):
        dims = [bits - 1 - b for b in group]
        own = [1 - ((me >> b) & 1) for b in group]
        def pick(code):
            out = buf
            for dim, b, o in zip(dims, group, own):
                flip = (code >> group.index(b)) & 1
                out = lax.dynamic_slice_in_dim(out, o ^ flip, 1, dim)
            return out
        acc = pick(0)
        for code in range(1, 1 << len(group)):
            mask = 0
            for k, b in enumerate(group):
                if (code >> k) & 1:
                    mask |= 1 << b
            acc = acc + lax.ppermute(pick(code), axis, partner_route(n, mask))
        buf = hook(acc)
    return jnp.flip(buf.reshape(pair, chans), 0)


def total_sum(value, axes):
    n = 1
    for name in axes:
        n *= lax.axis_size(name)
    terms = lax.all_to_all(jnp.broadcast_to(value, (n, 128)), axes, 0, 0, tiled=True)
    return jnp.sum(terms[:, 0])


def body(query_proj, key_proj, value_proj, filt_taps, grad_out):
    rows, chans = query_proj.shape
    reach = filt_taps.shape[0] - 1
    gated = (key_proj.astype(jnp.float32) * value_proj.astype(jnp.float32)).astype(jnp.bfloat16)
    scaled = (grad_out.astype(jnp.float32) * query_proj.astype(jnp.float32)).astype(jnp.bfloat16)
    before = shifted(gated[rows - reach :], "seq", 1)
    after = shifted(scaled[:reach], "seq", -1)
    gated_pad = jnp.concatenate([before, gated], 0).astype(jnp.float32)
    scaled_pad = jnp.concatenate([scaled, after], 0).astype(jnp.float32)
    local_sum = corr_part(gated_pad, scaled.astype(jnp.float32))
    pieces = 4
    width = chans // pieces
    work = [("q", p) for p in range(pieces)] + [("kv", p) for p in range(pieces)]
    done = {"q": [], "kv": []}

    def run_next(state):
        if not work:
            return state
        kind, p = work.pop(0)
        cols = slice(p * width, (p + 1) * width)
        pad = gated_pad if kind == "q" else scaled_pad
        state, pad, filt = lax.optimization_barrier((state, pad[:, cols], filt_taps[:, cols]))
        if kind == "q":
            filtered = causal_part(pad, filt)
            done["q"].append((grad_out[:, cols].astype(jnp.float32) * filtered).astype(jnp.bfloat16))
        else:
            grad_gated = anti_part(pad, filt)
            done["kv"].append((
                (grad_gated * value_proj[:, cols].astype(jnp.float32)).astype(jnp.bfloat16),
                (grad_gated * key_proj[:, cols].astype(jnp.float32)).astype(jnp.bfloat16),
            ))
        return state

    local_sum = run_next(local_sum)
    portion = scatter_sum(local_sum, "seq", run_next)
    entries = filt_taps.shape[0] * chans * lax.axis_size("chan")
    while work:
        portion = run_next(portion)
    squares = total_sum(jnp.sum(portion * portion), ("seq", "chan"))
    grad_q = jnp.concatenate(done["q"], 1)
    grad_k = jnp.concatenate([k for k, _ in done["kv"]], 1)
    grad_v = jnp.concatenate([v for _, v in done["kv"]], 1)
    grad_rms = jnp.sqrt(squares / entries + 1e-06)
    grad_filt = portion * jnp.minimum(1.0, 1.0 / grad_rms)
    return (grad_q, grad_k, grad_v, grad_filt)


def solution(mesh):
    placed = (
        P("seq", "chan"),
        P("seq", "chan"),
        P("seq", "chan"),
        P(None, "chan"),
        P("seq", "chan"),
    )
    return jax.shard_map(
        body,
        mesh=mesh,
        in_specs=placed,
        out_specs=(P("seq", "chan"), P("seq", "chan"), P("seq", "chan"), P("seq", "chan")),
        check_vma=False,
    )
```

```python
import jax
import jax.numpy as jnp
from jax import lax
from jax.sharding import PartitionSpec as P


def shifted(block, axis, distance):
    devices = range(lax.axis_size(axis))
    route = [(i - distance, i) for i in devices if i - distance in devices]
    return lax.ppermute(block, axis, route)


def causal_part(padded, filt):
    width = padded.shape[1]
    out = lax.conv_general_dilated(
        padded[None],
        jnp.flip(filt, 0)[:, None, :],
        (1,),
        "VALID",
        dimension_numbers=("NWC", "WIO", "NWC"),
        feature_group_count=width,
        precision=lax.Precision.HIGHEST,
    )
    return out[0]


def anti_part(padded, filt):
    width = padded.shape[1]
    out = lax.conv_general_dilated(
        padded[None],
        filt[:, None, :],
        (1,),
        "VALID",
        dimension_numbers=("NWC", "WIO", "NWC"),
        feature_group_count=width,
        precision=lax.Precision.HIGHEST,
    )
    return out[0]


def corr_part(padded, kernel):
    width = padded.shape[1]
    out = lax.conv_general_dilated(
        padded[None],
        kernel[:, None, :],
        (1,),
        "VALID",
        dimension_numbers=("NWC", "WIO", "NWC"),
        feature_group_count=width,
        precision=lax.Precision.HIGHEST,
    )
    return out[0]


def group_rounds(axis_bits):
    return [[b] for b in range(axis_bits)]


def partner_route(n, mask):
    return [(j, j ^ mask) for j in range(n)]


def scatter_sum(rows_rev, axis, hook):
    n = lax.axis_size(axis)
    bits = n.bit_length() - 1
    me = lax.axis_index(axis)
    chans = rows_rev.shape[1]
    pair = rows_rev.shape[0] // n
    buf = rows_rev.reshape((2,) * bits + (pair, chans))
    for group in group_rounds(bits):
        dims = [bits - 1 - b for b in group]
        own = [1 - ((me >> b) & 1) for b in group]
        def pick(code):
            out = buf
            for dim, b, o in zip(dims, group, own):
                flip = (code >> group.index(b)) & 1
                out = lax.dynamic_slice_in_dim(out, o ^ flip, 1, dim)
            return out
        acc = pick(0)
        for code in range(1, 1 << len(group)):
            mask = 0
            for k, b in enumerate(group):
                if (code >> k) & 1:
                    mask |= 1 << b
            acc = acc + lax.ppermute(pick(code), axis, partner_route(n, mask))
        buf = hook(acc)
    return jnp.flip(buf.reshape(pair, chans), 0)


def total_sum(value, axes):
    n = 1
    for name in axes:
        n *= lax.axis_size(name)
    terms = lax.all_to_all(jnp.broadcast_to(value, (n, 128)), axes, 0, 0, tiled=True)
    return jnp.sum(terms[:, 0])


def body(query_proj, key_proj, value_proj, filt_taps, grad_out):
    rows, chans = query_proj.shape
    reach = filt_taps.shape[0] - 1
    gated = (key_proj.astype(jnp.float32) * value_proj.astype(jnp.float32)).astype(jnp.bfloat16)
    scaled = (grad_out.astype(jnp.float32) * query_proj.astype(jnp.float32)).astype(jnp.bfloat16)
    before = shifted(gated[rows - reach :], "seq", 1)
    after = shifted(scaled[:reach], "seq", -1)
    gated_pad = jnp.concatenate([before, gated], 0).astype(jnp.float32)
    scaled_pad = jnp.concatenate([scaled, after], 0).astype(jnp.float32)
    local_sum = corr_part(gated_pad, scaled.astype(jnp.float32))
    pieces = 4
    width = chans // pieces
    work = [("q", p) for p in range(pieces)] + [("kv", p) for p in range(pieces)]
    taps_n = filt_taps.shape[0]
    lane = lax.broadcasted_iota(jnp.int32, (taps_n, taps_n), 1)
    row = lax.broadcasted_iota(jnp.int32, (taps_n, taps_n), 0)
    exchange = (lane + row == taps_n - 1).astype(jnp.float32)
    flipped = jnp.dot(exchange, filt_taps, precision=lax.Precision.HIGHEST)
    done = {"q": [], "kv": []}

    def run_next(state):
        if not work:
            return state
        kind, p = work.pop(0)
        cols = slice(p * width, (p + 1) * width)
        pad, taps = (gated_pad, flipped) if kind == "q" else (scaled_pad, filt_taps)
        state, pad, filt = lax.optimization_barrier((state, pad[:, cols], taps[:, cols]))
        if kind == "q":
            filtered = anti_part(pad, filt)
            done["q"].append((grad_out[:, cols].astype(jnp.float32) * filtered).astype(jnp.bfloat16))
        else:
            grad_gated = anti_part(pad, filt)
            done["kv"].append((
                (grad_gated * value_proj[:, cols].astype(jnp.float32)).astype(jnp.bfloat16),
                (grad_gated * key_proj[:, cols].astype(jnp.float32)).astype(jnp.bfloat16),
            ))
        return state

    local_sum = run_next(local_sum)
    portion = scatter_sum(local_sum, "seq", run_next)
    entries = filt_taps.shape[0] * chans * lax.axis_size("chan")
    while work:
        portion = run_next(portion)
    squares = total_sum(jnp.sum(portion * portion), ("seq", "chan"))
    grad_q = jnp.concatenate(done["q"], 1)
    grad_k = jnp.concatenate([k for k, _ in done["kv"]], 1)
    grad_v = jnp.concatenate([v for _, v in done["kv"]], 1)
    grad_rms = jnp.sqrt(squares / entries + 1e-06)
    grad_filt = portion * jnp.minimum(1.0, 1.0 / grad_rms)
    return (grad_q, grad_k, grad_v, grad_filt)


def solution(mesh):
    placed = (
        P("seq", "chan"),
        P("seq", "chan"),
        P("seq", "chan"),
        P(None, "chan"),
        P("seq", "chan"),
    )
    return jax.shard_map(
        body,
        mesh=mesh,
        in_specs=placed,
        out_specs=(P("seq", "chan"), P("seq", "chan"), P("seq", "chan"), P("seq", "chan")),
        check_vma=False,
    )
```

```python
import jax
import jax.numpy as jnp
from jax import lax
from jax.sharding import PartitionSpec as P


def shifted(block, axis, distance):
    devices = range(lax.axis_size(axis))
    route = [(i - distance, i) for i in devices if i - distance in devices]
    return lax.ppermute(block, axis, route)


def causal_part(padded, filt):
    width = padded.shape[1]
    out = lax.conv_general_dilated(
        padded[None],
        jnp.flip(filt, 0)[:, None, :],
        (1,),
        "VALID",
        dimension_numbers=("NWC", "WIO", "NWC"),
        feature_group_count=width,
        precision=lax.Precision.HIGHEST,
    )
    return out[0]


def anti_part(padded, filt):
    width = padded.shape[1]
    out = lax.conv_general_dilated(
        padded[None],
        filt[:, None, :],
        (1,),
        "VALID",
        dimension_numbers=("NWC", "WIO", "NWC"),
        feature_group_count=width,
        precision=lax.Precision.HIGHEST,
    )
    return out[0]


def corr_part(padded, kernel):
    width = padded.shape[1]
    out = lax.conv_general_dilated(
        padded[None],
        kernel[:, None, :],
        (1,),
        "VALID",
        dimension_numbers=("NWC", "WIO", "NWC"),
        feature_group_count=width,
        precision=lax.Precision.HIGHEST,
    )
    return out[0]


def group_rounds(axis_bits):
    return [[b] for b in range(axis_bits)]


def partner_route(n, mask):
    return [(j, j ^ mask) for j in range(n)]


def scatter_sum(rows_rev, axis, hook):
    n = lax.axis_size(axis)
    bits = n.bit_length() - 1
    me = lax.axis_index(axis)
    chans = rows_rev.shape[1]
    pair = rows_rev.shape[0] // n
    buf = rows_rev.reshape((2,) * bits + (pair, chans))
    for group in group_rounds(bits):
        dims = [bits - 1 - b for b in group]
        own = [1 - ((me >> b) & 1) for b in group]
        def pick(code):
            out = buf
            for dim, b, o in zip(dims, group, own):
                flip = (code >> group.index(b)) & 1
                out = lax.dynamic_slice_in_dim(out, o ^ flip, 1, dim)
            return out
        acc = pick(0)
        for code in range(1, 1 << len(group)):
            mask = 0
            for k, b in enumerate(group):
                if (code >> k) & 1:
                    mask |= 1 << b
            acc = acc + lax.ppermute(pick(code), axis, partner_route(n, mask))
        buf = hook(acc)
    return jnp.flip(buf.reshape(pair, chans), 0)


def total_sum(value, axes):
    n = 1
    for name in axes:
        n *= lax.axis_size(name)
    terms = lax.all_to_all(jnp.broadcast_to(value, (n, 128)), axes, 0, 0, tiled=True)
    return jnp.sum(terms[:, 0])


def body(query_proj, key_proj, value_proj, filt_taps, grad_out):
    rows, chans = query_proj.shape
    reach = filt_taps.shape[0] - 1
    gated = (key_proj.astype(jnp.float32) * value_proj.astype(jnp.float32)).astype(jnp.bfloat16)
    scaled = (grad_out.astype(jnp.float32) * query_proj.astype(jnp.float32)).astype(jnp.bfloat16)
    before = shifted(gated[rows - reach :], "seq", 1)
    after = shifted(scaled[:reach], "seq", -1)
    gated_pad = jnp.concatenate([before, gated], 0).astype(jnp.float32)
    scaled_pad = jnp.concatenate([scaled, after], 0).astype(jnp.float32)
    half = rows // 2
    scaled_wide = scaled.astype(jnp.float32)
    local_sum = corr_part(gated_pad[: half + reach], scaled_wide[:half]) + corr_part(
        gated_pad[half:], scaled_wide[half:]
    )
    pieces = 4
    width = chans // pieces
    work = [("q", p) for p in range(pieces)] + [("kv", p) for p in range(pieces)]
    taps_n = filt_taps.shape[0]
    lane = lax.broadcasted_iota(jnp.int32, (taps_n, taps_n), 1)
    row = lax.broadcasted_iota(jnp.int32, (taps_n, taps_n), 0)
    exchange = (lane + row == taps_n - 1).astype(jnp.float32)
    flipped = jnp.dot(exchange, filt_taps, precision=lax.Precision.HIGHEST)
    done = {"q": [], "kv": []}

    def run_next(state):
        if not work:
            return state
        kind, p = work.pop(0)
        cols = slice(p * width, (p + 1) * width)
        pad, taps = (gated_pad, flipped) if kind == "q" else (scaled_pad, filt_taps)
        state, pad, filt = lax.optimization_barrier((state, pad[:, cols], taps[:, cols]))
        if kind == "q":
            filtered = anti_part(pad, filt)
            done["q"].append((grad_out[:, cols].astype(jnp.float32) * filtered).astype(jnp.bfloat16))
        else:
            grad_gated = anti_part(pad, filt)
            done["kv"].append((
                (grad_gated * value_proj[:, cols].astype(jnp.float32)).astype(jnp.bfloat16),
                (grad_gated * key_proj[:, cols].astype(jnp.float32)).astype(jnp.bfloat16),
            ))
        return state

    local_sum = run_next(local_sum)
    portion = scatter_sum(local_sum, "seq", run_next)
    entries = filt_taps.shape[0] * chans * lax.axis_size("chan")
    while work:
        portion = run_next(portion)
    squares = total_sum(jnp.sum(portion * portion), ("seq", "chan"))
    grad_q = jnp.concatenate(done["q"], 1)
    grad_k = jnp.concatenate([k for k, _ in done["kv"]], 1)
    grad_v = jnp.concatenate([v for _, v in done["kv"]], 1)
    grad_rms = jnp.sqrt(squares / entries + 1e-06)
    grad_filt = portion * jnp.minimum(1.0, 1.0 / grad_rms)
    return (grad_q, grad_k, grad_v, grad_filt)


def solution(mesh):
    placed = (
        P("seq", "chan"),
        P("seq", "chan"),
        P("seq", "chan"),
        P(None, "chan"),
        P("seq", "chan"),
    )
    return jax.shard_map(
        body,
        mesh=mesh,
        in_specs=placed,
        out_specs=(P("seq", "chan"), P("seq", "chan"), P("seq", "chan"), P("seq", "chan")),
        check_vma=False,
    )
```

```python
import jax
import jax.numpy as jnp
from jax import lax
from jax.sharding import PartitionSpec as P


def shifted(block, axis, distance):
    devices = range(lax.axis_size(axis))
    route = [(i - distance, i) for i in devices if i - distance in devices]
    return lax.ppermute(block, axis, route)


def causal_part(padded, filt):
    width = padded.shape[1]
    out = lax.conv_general_dilated(
        padded[None],
        jnp.flip(filt, 0)[:, None, :],
        (1,),
        "VALID",
        dimension_numbers=("NWC", "WIO", "NWC"),
        feature_group_count=width,
        precision=lax.Precision.HIGHEST,
    )
    return out[0]


def anti_part(padded, filt):
    width = padded.shape[1]
    out = lax.conv_general_dilated(
        padded[None],
        filt[:, None, :],
        (1,),
        "VALID",
        dimension_numbers=("NWC", "WIO", "NWC"),
        feature_group_count=width,
        precision=lax.Precision.HIGHEST,
    )
    return out[0]


def corr_part(padded, kernel):
    width = padded.shape[1]
    out = lax.conv_general_dilated(
        padded[None],
        kernel[:, None, :],
        (1,),
        "VALID",
        dimension_numbers=("NWC", "WIO", "NWC"),
        feature_group_count=width,
        precision=lax.Precision.HIGHEST,
    )
    return out[0]


def group_rounds(axis_bits):
    return [[b] for b in range(axis_bits)]


def partner_route(n, mask):
    return [(j, j ^ mask) for j in range(n)]


def scatter_sum(rows_rev, axis, hook):
    n = lax.axis_size(axis)
    bits = n.bit_length() - 1
    me = lax.axis_index(axis)
    chans = rows_rev.shape[1]
    pair = rows_rev.shape[0] // n
    buf = rows_rev.reshape((2,) * bits + (pair, chans))
    for group in group_rounds(bits):
        dims = [bits - 1 - b for b in group]
        own = [1 - ((me >> b) & 1) for b in group]
        def pick(code):
            out = buf
            for dim, b, o in zip(dims, group, own):
                flip = (code >> group.index(b)) & 1
                out = lax.dynamic_slice_in_dim(out, o ^ flip, 1, dim)
            return out
        acc = pick(0)
        for code in range(1, 1 << len(group)):
            mask = 0
            for k, b in enumerate(group):
                if (code >> k) & 1:
                    mask |= 1 << b
            acc = acc + lax.ppermute(pick(code), axis, partner_route(n, mask))
        buf = hook(acc)
    return jnp.flip(buf.reshape(pair, chans), 0)


def total_sum(value, axes):
    n = 1
    for name in axes:
        n *= lax.axis_size(name)
    terms = lax.all_to_all(jnp.broadcast_to(value, (n, 128)), axes, 0, 0, tiled=True)
    return jnp.sum(terms[:, 0])


def body(query_proj, key_proj, value_proj, filt_taps, grad_out):
    rows, chans = query_proj.shape
    reach = filt_taps.shape[0] - 1
    gated = (key_proj.astype(jnp.float32) * value_proj.astype(jnp.float32)).astype(jnp.bfloat16)
    scaled = (grad_out.astype(jnp.float32) * query_proj.astype(jnp.float32)).astype(jnp.bfloat16)
    tail = (key_proj[rows - reach :].astype(jnp.float32) * value_proj[rows - reach :].astype(jnp.float32))
    head = (grad_out[:reach].astype(jnp.float32) * query_proj[:reach].astype(jnp.float32))
    before = shifted(tail.astype(jnp.bfloat16), "seq", 1)
    after = shifted(head.astype(jnp.bfloat16), "seq", -1)
    gated_pad = jnp.concatenate([before, gated], 0).astype(jnp.float32)
    scaled_pad = jnp.concatenate([scaled, after], 0).astype(jnp.float32)
    local_sum = corr_part(gated_pad, scaled.astype(jnp.float32))
    pieces = 4
    width = chans // pieces
    work = [("q", p) for p in range(pieces)] + [("kv", p) for p in range(pieces)]
    taps_n = filt_taps.shape[0]
    lane = lax.broadcasted_iota(jnp.int32, (taps_n, taps_n), 1)
    row = lax.broadcasted_iota(jnp.int32, (taps_n, taps_n), 0)
    exchange = (lane + row == taps_n - 1).astype(jnp.float32)
    flipped = jnp.dot(exchange, filt_taps, precision=lax.Precision.HIGHEST)
    outs = {name: jnp.zeros((rows, chans), jnp.bfloat16) for name in ("q", "k", "v")}

    def run_next(state):
        if not work:
            return state
        kind, p = work.pop(0)
        cols = slice(p * width, (p + 1) * width)
        pad, taps = (gated_pad, flipped) if kind == "q" else (scaled_pad, filt_taps)
        state, pad, filt = lax.optimization_barrier((state, pad[:, cols], taps[:, cols]))
        if kind == "q":
            filtered = anti_part(pad, filt)
            outs["q"] = outs["q"].at[:, cols].set((grad_out[:, cols].astype(jnp.float32) * filtered).astype(jnp.bfloat16))
        else:
            grad_gated = anti_part(pad, filt)
            outs["k"] = outs["k"].at[:, cols].set((grad_gated * value_proj[:, cols].astype(jnp.float32)).astype(jnp.bfloat16))
            outs["v"] = outs["v"].at[:, cols].set((grad_gated * key_proj[:, cols].astype(jnp.float32)).astype(jnp.bfloat16))
        return state

    local_sum = run_next(local_sum)
    portion = scatter_sum(local_sum, "seq", run_next)
    entries = filt_taps.shape[0] * chans * lax.axis_size("chan")
    while work:
        portion = run_next(portion)
    squares = total_sum(jnp.sum(portion * portion), ("seq", "chan"))
    grad_q, grad_k, grad_v = outs["q"], outs["k"], outs["v"]
    grad_rms = jnp.sqrt(squares / entries + 1e-06)
    grad_filt = portion * jnp.minimum(1.0, 1.0 / grad_rms)
    return (grad_q, grad_k, grad_v, grad_filt)


def solution(mesh):
    placed = (
        P("seq", "chan"),
        P("seq", "chan"),
        P("seq", "chan"),
        P(None, "chan"),
        P("seq", "chan"),
    )
    return jax.shard_map(
        body,
        mesh=mesh,
        in_specs=placed,
        out_specs=(P("seq", "chan"), P("seq", "chan"), P("seq", "chan"), P("seq", "chan")),
        check_vma=False,
    )
```

```python
import jax
import jax.numpy as jnp
from jax import lax
from jax.sharding import PartitionSpec as P


def shifted(block, axis, distance):
    devices = range(lax.axis_size(axis))
    route = [(i - distance, i) for i in devices if i - distance in devices]
    return lax.ppermute(block, axis, route)


def causal_part(padded, filt):
    width = padded.shape[1]
    out = lax.conv_general_dilated(
        padded[None],
        jnp.flip(filt, 0)[:, None, :],
        (1,),
        "VALID",
        dimension_numbers=("NWC", "WIO", "NWC"),
        feature_group_count=width,
        precision=lax.Precision.HIGHEST,
    )
    return out[0]


def anti_part(padded, filt):
    width = padded.shape[1]
    out = lax.conv_general_dilated(
        padded[None],
        filt[:, None, :],
        (1,),
        "VALID",
        dimension_numbers=("NWC", "WIO", "NWC"),
        feature_group_count=width,
        precision=lax.Precision.HIGHEST,
    )
    return out[0]


def corr_part(padded, kernel):
    width = padded.shape[1]
    out = lax.conv_general_dilated(
        padded[None],
        kernel[:, None, :],
        (1,),
        "VALID",
        dimension_numbers=("NWC", "WIO", "NWC"),
        feature_group_count=width,
        precision=lax.Precision.HIGHEST,
    )
    return out[0]


def group_rounds(axis_bits):
    return [[b] for b in range(axis_bits)]


def partner_route(n, mask):
    return [(j, j ^ mask) for j in range(n)]


def scatter_sum(rows_rev, axis, hook):
    n = lax.axis_size(axis)
    bits = n.bit_length() - 1
    me = lax.axis_index(axis)
    chans = rows_rev.shape[1]
    pair = rows_rev.shape[0] // n
    buf = rows_rev.reshape((2,) * bits + (pair, chans))
    for group in group_rounds(bits):
        dims = [bits - 1 - b for b in group]
        own = [1 - ((me >> b) & 1) for b in group]
        def pick(code):
            out = buf
            for dim, b, o in zip(dims, group, own):
                flip = (code >> group.index(b)) & 1
                out = lax.dynamic_slice_in_dim(out, o ^ flip, 1, dim)
            return out
        acc = pick(0)
        for code in range(1, 1 << len(group)):
            mask = 0
            for k, b in enumerate(group):
                if (code >> k) & 1:
                    mask |= 1 << b
            acc = acc + lax.ppermute(pick(code), axis, partner_route(n, mask))
        buf = hook(acc)
    return jnp.flip(buf.reshape(pair, chans), 0)


def total_sum(value, axes):
    n = 1
    for name in axes:
        n *= lax.axis_size(name)
    terms = lax.all_to_all(jnp.broadcast_to(value, (n, 128)), axes, 0, 0, tiled=True)
    return jnp.sum(terms[:, 0])


def body(query_proj, key_proj, value_proj, filt_taps, grad_out):
    rows, chans = query_proj.shape
    reach = filt_taps.shape[0] - 1
    gated = (key_proj.astype(jnp.float32) * value_proj.astype(jnp.float32)).astype(jnp.bfloat16)
    scaled = (grad_out.astype(jnp.float32) * query_proj.astype(jnp.float32)).astype(jnp.bfloat16)
    before = shifted(gated[rows - reach :], "seq", 1)
    after = shifted(scaled[:reach], "seq", -1)
    gated_pad = jnp.concatenate([before, gated], 0).astype(jnp.float32)
    scaled_pad = jnp.concatenate([scaled, after], 0).astype(jnp.float32)
    local_sum = corr_part(gated_pad, scaled.astype(jnp.float32))
    pieces = 4
    width = chans // pieces
    work = [(kind, p) for p in range(pieces) for kind in ("kv", "q")]
    taps_n = filt_taps.shape[0]
    lane = lax.broadcasted_iota(jnp.int32, (taps_n, taps_n), 1)
    row = lax.broadcasted_iota(jnp.int32, (taps_n, taps_n), 0)
    exchange = (lane + row == taps_n - 1).astype(jnp.float32)
    flipped = jnp.dot(exchange, filt_taps, precision=lax.Precision.HIGHEST)
    done = {"q": [], "kv": []}

    def run_next(state):
        if not work:
            return state
        kind, p = work.pop(0)
        cols = slice(p * width, (p + 1) * width)
        pad, taps = (gated_pad, flipped) if kind == "q" else (scaled_pad, filt_taps)
        state, pad, filt = lax.optimization_barrier((state, pad[:, cols], taps[:, cols]))
        if kind == "q":
            filtered = anti_part(pad, filt)
            done["q"].append((grad_out[:, cols].astype(jnp.float32) * filtered).astype(jnp.bfloat16))
        else:
            grad_gated = anti_part(pad, filt)
            done["kv"].append((
                (grad_gated * value_proj[:, cols].astype(jnp.float32)).astype(jnp.bfloat16),
                (grad_gated * key_proj[:, cols].astype(jnp.float32)).astype(jnp.bfloat16),
            ))
        return state

    local_sum = run_next(local_sum)
    portion = scatter_sum(local_sum, "seq", run_next)
    entries = filt_taps.shape[0] * chans * lax.axis_size("chan")
    while work:
        portion = run_next(portion)
    squares = total_sum(jnp.sum(portion * portion), ("seq", "chan"))
    grad_q = jnp.concatenate(done["q"], 1)
    grad_k = jnp.concatenate([k for k, _ in done["kv"]], 1)
    grad_v = jnp.concatenate([v for _, v in done["kv"]], 1)
    grad_rms = jnp.sqrt(squares / entries + 1e-06)
    grad_filt = portion * jnp.minimum(1.0, 1.0 / grad_rms)
    return (grad_q, grad_k, grad_v, grad_filt)


def solution(mesh):
    placed = (
        P("seq", "chan"),
        P("seq", "chan"),
        P("seq", "chan"),
        P(None, "chan"),
        P("seq", "chan"),
    )
    return jax.shard_map(
        body,
        mesh=mesh,
        in_specs=placed,
        out_specs=(P("seq", "chan"), P("seq", "chan"), P("seq", "chan"), P("seq", "chan")),
        check_vma=False,
    )
```

```python
import jax
import jax.numpy as jnp
from jax import lax
from jax.sharding import PartitionSpec as P


def shifted(block, axis, distance):
    devices = range(lax.axis_size(axis))
    route = [(i - distance, i) for i in devices if i - distance in devices]
    return lax.ppermute(block, axis, route)


def causal_part(padded, filt):
    width = padded.shape[1]
    out = lax.conv_general_dilated(
        padded[None],
        jnp.flip(filt, 0)[:, None, :],
        (1,),
        "VALID",
        dimension_numbers=("NWC", "WIO", "NWC"),
        feature_group_count=width,
        precision=lax.Precision.HIGHEST,
    )
    return out[0]


def anti_part(padded, filt):
    width = padded.shape[1]
    out = lax.conv_general_dilated(
        padded[None],
        filt[:, None, :],
        (1,),
        "VALID",
        dimension_numbers=("NWC", "WIO", "NWC"),
        feature_group_count=width,
        precision=lax.Precision.HIGHEST,
    )
    return out[0]


def corr_part(padded, kernel):
    width = padded.shape[1]
    out = lax.conv_general_dilated(
        padded[None],
        kernel[:, None, :],
        (1,),
        "VALID",
        dimension_numbers=("NWC", "WIO", "NWC"),
        feature_group_count=width,
        precision=lax.Precision.HIGHEST,
    )
    return out[0]


def group_rounds(axis_bits):
    return [[b] for b in range(axis_bits)]


def partner_route(n, mask):
    return [(j, j ^ mask) for j in range(n)]


def scatter_sum(rows_rev, axis, hook):
    n = lax.axis_size(axis)
    bits = n.bit_length() - 1
    me = lax.axis_index(axis)
    chans = rows_rev.shape[1]
    pair = rows_rev.shape[0] // n
    buf = rows_rev.reshape((2,) * bits + (pair, chans))
    for group in group_rounds(bits):
        dims = [bits - 1 - b for b in group]
        own = [1 - ((me >> b) & 1) for b in group]
        def pick(code):
            out = buf
            for dim, b, o in zip(dims, group, own):
                flip = (code >> group.index(b)) & 1
                out = lax.dynamic_slice_in_dim(out, o ^ flip, 1, dim)
            return out
        acc = pick(0)
        for code in range(1, 1 << len(group)):
            mask = 0
            for k, b in enumerate(group):
                if (code >> k) & 1:
                    mask |= 1 << b
            acc = acc + lax.ppermute(pick(code), axis, partner_route(n, mask))
        buf = hook(acc)
    return buf.reshape(pair, chans)


def total_sum(value, axes):
    n = 1
    for name in axes:
        n *= lax.axis_size(name)
    terms = lax.all_to_all(jnp.broadcast_to(value, (n, 128)), axes, 0, 0, tiled=True)
    return jnp.sum(terms[:, 0])


def body(query_proj, key_proj, value_proj, filt_taps, grad_out):
    rows, chans = query_proj.shape
    reach = filt_taps.shape[0] - 1
    gated = (key_proj.astype(jnp.float32) * value_proj.astype(jnp.float32)).astype(jnp.bfloat16)
    scaled = (grad_out.astype(jnp.float32) * query_proj.astype(jnp.float32)).astype(jnp.bfloat16)
    before = shifted(gated[rows - reach :], "seq", 1)
    after = shifted(scaled[:reach], "seq", -1)
    gated_pad = jnp.concatenate([before, gated], 0).astype(jnp.float32)
    scaled_pad = jnp.concatenate([scaled, after], 0).astype(jnp.float32)
    local_sum = corr_part(gated_pad, scaled.astype(jnp.float32))
    pieces = 4
    width = chans // pieces
    work = [("q", p) for p in range(pieces)] + [("kv", p) for p in range(pieces)]
    taps_n = filt_taps.shape[0]
    lane = lax.broadcasted_iota(jnp.int32, (taps_n, taps_n), 1)
    row = lax.broadcasted_iota(jnp.int32, (taps_n, taps_n), 0)
    exchange = (lane + row == taps_n - 1).astype(jnp.float32)
    flipped = jnp.dot(exchange, filt_taps, precision=lax.Precision.HIGHEST)
    done = {"q": [], "kv": []}

    def run_next(state):
        if not work:
            return state
        kind, p = work.pop(0)
        cols = slice(p * width, (p + 1) * width)
        pad, taps = (gated_pad, flipped) if kind == "q" else (scaled_pad, filt_taps)
        state, pad, filt = lax.optimization_barrier((state, pad[:, cols], taps[:, cols]))
        if kind == "q":
            filtered = anti_part(pad, filt)
            done["q"].append((grad_out[:, cols].astype(jnp.float32) * filtered).astype(jnp.bfloat16))
        else:
            grad_gated = anti_part(pad, filt)
            done["kv"].append((
                (grad_gated * value_proj[:, cols].astype(jnp.float32)).astype(jnp.bfloat16),
                (grad_gated * key_proj[:, cols].astype(jnp.float32)).astype(jnp.bfloat16),
            ))
        return state

    local_sum = run_next(local_sum)
    portion = scatter_sum(local_sum, "seq", run_next)
    entries = filt_taps.shape[0] * chans * lax.axis_size("chan")
    while work:
        portion = run_next(portion)
    squares = total_sum(jnp.sum(portion * portion), ("seq", "chan"))
    portion = jnp.concatenate([portion[1:], portion[:1]], 0)
    grad_q = jnp.concatenate(done["q"], 1)
    grad_k = jnp.concatenate([k for k, _ in done["kv"]], 1)
    grad_v = jnp.concatenate([v for _, v in done["kv"]], 1)
    grad_rms = jnp.sqrt(squares / entries + 1e-06)
    grad_filt = portion * jnp.minimum(1.0, 1.0 / grad_rms)
    return (grad_q, grad_k, grad_v, grad_filt)


def solution(mesh):
    placed = (
        P("seq", "chan"),
        P("seq", "chan"),
        P("seq", "chan"),
        P(None, "chan"),
        P("seq", "chan"),
    )
    return jax.shard_map(
        body,
        mesh=mesh,
        in_specs=placed,
        out_specs=(P("seq", "chan"), P("seq", "chan"), P("seq", "chan"), P("seq", "chan")),
        check_vma=False,
    )
```
